32 devices in a mesh: dp: 4 (over y, core), mp: 8 (over z, x).
Axes of the slice: x: 2, y: 2, z: 4, core: 2. Of those that a mesh axis runs over, the one named last changes fastest.
Arguments:
- grad_part: bfloat16 [4, 24, 512, 512], P('dp', None, 'mp'), may hold values from -3 to 3
- owner: int32 [4, 6], replicated, may hold values from 0 to 7, as said below
- moment: bfloat16 [24, 512, 512], P('dp', 'mp'), may hold values from -6 to 6
- gram_left: bfloat16 [4, 8, 2, 512, 512], P('dp', 'mp'), may hold values from -1 to 7, as said below
- gram_right: bfloat16 [4, 8, 2, 512, 512], P('dp', 'mp'), may hold values from -1 to 7, as said below
- basis_left: bfloat16 [4, 8, 2, 512, 512], P('dp', 'mp'), may hold values from -1 to 2, as said below
- basis_right: bfloat16 [4, 8, 2, 512, 512], P('dp', 'mp'), may hold values from -1 to 2, as said below
Outputs:
- gram_left_new: bfloat16 [4, 8, 2, 512, 512], P('dp', 'mp')
- gram_right_new: bfloat16 [4, 8, 2, 512, 512], P('dp', 'mp')
- basis_left_new: bfloat16 [4, 8, 2, 512, 512], P('dp', 'mp')
- basis_right_new: bfloat16 [4, 8, 2, 512, 512], P('dp', 'mp')
- moment_new: bfloat16 [24, 512, 512], P('dp', 'mp')
The draws below stay inside these ranges and needn't reach their ends.
Inputs may be any that keep to these rules, and one draw needn't show every extreme that they name: In every row, owners 2i and 2i + 1 together own at most 2 blocks, and some owner owns exactly 2 blocks. `gram_left`: each slot is symmetric positive definite. `gram_right`: each slot is symmetric positive definite. `basis_left`: each slot is nonsingular. `basis_right`: each slot is nonsingular.
All inputs are finite; a program needn't handle non-finite values.
Results may differ from the reference program's by a relative error of at most 0.008.
Values may be sent and summed in bfloat16 or wider, within the bound.
No kernel may reach another device: no remote copies, remote signals or barrier semaphores. Data moves between devices by JAX's collectives and lax.ppermute only.
A program may use at most 128 MiB of HBM per device.

```python
import math
import jax
import jax.numpy as jnp
from jax import lax

BS = 512
CAP = 2
BLOCKS_PER_GROUP = 6
NB = 24
N_DP = 4
N_MP = 8


def one_table(table_key):
    key_order, key_rest, key_bits = jax.random.split(table_key, 3)
    pairing_sequence = jax.random.permutation(key_order, N_MP // 2)
    remaining_slots = 2 + jax.random.permutation(key_rest, N_MP - 2)
    renamed_labels = jnp.concatenate([jnp.array([0, 1], jnp.int32), remaining_slots[:BLOCKS_PER_GROUP - 2].astype(jnp.int32)])
    pair_lookup = pairing_sequence[renamed_labels // 2].astype(jnp.int32)
    owner_bits = jax.random.randint(key_bits, (BLOCKS_PER_GROUP,), 0, 2).astype(jnp.int32)
    owner_bits = owner_bits.at[1].set(owner_bits[0])
    return (2 * pair_lookup + owner_bits).astype(jnp.int32)


def draw_owner(key, part):
    table_keys = jax.random.split(jax.random.fold_in(key, 5), N_DP)
    return jax.vmap(one_table)(table_keys)


def symmetric_draw(state_key):
    full_shape = (N_DP, N_MP, CAP, BS, BS)
    key_diag, key_one = jax.random.split(state_key, 2)
    diagonal = jax.random.uniform(key_diag, full_shape[:4], jnp.float32, 2.5, 6.0)
    random_part = jax.random.uniform(key_one, full_shape, jnp.float32, -1.0, 1.0)
    spread = 1.0 / math.sqrt(BS) * (random_part + jnp.swapaxes(random_part, 3, 4))
    row_ids = lax.broadcasted_iota(jnp.int32, full_shape, 3)
    col_ids = lax.broadcasted_iota(jnp.int32, full_shape, 4)
    return jnp.where(row_ids == col_ids, diagonal[..., None], spread).astype(jnp.bfloat16)


def near_identity(state_key):
    full_shape = (N_DP, N_MP, CAP, BS, BS)
    key_one = jax.random.fold_in(state_key, 0)
    noise = 0.5 / math.sqrt(BS) * jax.random.uniform(key_one, full_shape, jnp.float32, -1.0, 1.0)
    row_ids = lax.broadcasted_iota(jnp.int32, full_shape, 3)
    col_ids = lax.broadcasted_iota(jnp.int32, full_shape, 4)
    identity = jnp.where(row_ids == col_ids, 1.0, 0.0).astype(jnp.float32)
    return (identity + noise).astype(jnp.bfloat16)


def draw_gram_left(key, part):
    return symmetric_draw(jax.random.fold_in(key, 1))


def draw_gram_right(key, part):
    return symmetric_draw(jax.random.fold_in(key, 2))


def draw_basis_left(key, part):
    return near_identity(jax.random.fold_in(key, 3))


def draw_basis_right(key, part):
    return near_identity(jax.random.fold_in(key, 4))


def block_levels(rng, dims, shards, smallest, top_value):
    level, own = 1.0, jax.random.fold_in(rng, 6)
    for axis_at, parts in shards:
        steps = jnp.exp(jax.random.uniform(jax.random.fold_in(own, axis_at), (parts,), jnp.float32, smallest / len(shards), top_value / len(shards)))
        level = level * jnp.repeat(steps, dims[axis_at] // parts).reshape([-1 if axis == axis_at else 1 for axis in range(len(dims))])
    return level


def normal_values(stream_key, dims, width, bound, cuts=(), dtype=jnp.bfloat16):
    level = block_levels(stream_key, dims, cuts, -0.22, 0.18) if cuts else 1.0
    result = jax.random.normal(stream_key, dims, jnp.float32) * width * level
    return jnp.minimum(jnp.maximum(result, -bound), bound).astype(dtype)


def setup_inputs(seed: int = 0) -> dict:
    key_list = jax.random.split(jax.random.key(seed), 8)
    return {
        "grad_part": normal_values(key_list[0], (N_DP, NB, BS, BS), 0.5, 3.0, ((0, 4), (2, 8))),
        "owner": draw_owner(jax.random.fold_in(key_list[7], 71), 0),
        "moment": normal_values(key_list[2], (NB, BS, BS), 1.0, 6.0, ((0, 4), (1, 8))),
        "gram_left": draw_gram_left(jax.random.fold_in(key_list[7], 71), 0),
        "gram_right": draw_gram_right(jax.random.fold_in(key_list[7], 71), 0),
        "basis_left": draw_basis_left(jax.random.fold_in(key_list[7], 71), 0),
        "basis_right": draw_basis_right(jax.random.fold_in(key_list[7], 71), 0),
    }


gram_decay = 0.85
moment_decay = 0.9

def slot_numbers(row):
    length = row.shape[0]
    equal_owner = row[:, None] == row[None, :]
    earlier = lax.broadcasted_iota(jnp.int32, (length, length), 1) < lax.broadcasted_iota(jnp.int32, (length, length), 0)
    return jnp.sum(jnp.where(equal_owner & earlier, 1, 0), axis=1).astype(jnp.int32)

def orthonormal(matrix_product):
    square = jnp.dot(matrix_product.T.astype(jnp.float32), matrix_product.astype(jnp.float32), precision=lax.Precision.HIGHEST, preferred_element_type=jnp.float32)
    factor = jnp.linalg.cholesky(square)
    solved = jax.scipy.linalg.solve_triangular(factor, matrix_product.T, lower=True)
    return solved.T.astype(jnp.bfloat16)

def refresh(left_gram, right_gram, left_old, right_old, gradient, moment):
    block_width = gradient.shape[0]
    outer_left = jnp.dot(gradient.astype(jnp.float32), gradient.T.astype(jnp.float32), preferred_element_type=jnp.float32)
    outer_right = jnp.dot(gradient.T.astype(jnp.float32), gradient.astype(jnp.float32), preferred_element_type=jnp.float32)
    left_stat = (gram_decay * left_gram.astype(jnp.float32) + (1.0 - gram_decay) / block_width * outer_left).astype(jnp.bfloat16)
    right_statistic = (gram_decay * right_gram.astype(jnp.float32) + (1.0 - gram_decay) / block_width * outer_right).astype(jnp.bfloat16)
    left_basis = orthonormal(jnp.dot(left_stat.astype(jnp.float32), left_old.astype(jnp.float32), preferred_element_type=jnp.float32))
    right_basis = orthonormal(jnp.dot(right_statistic.astype(jnp.float32), right_old.astype(jnp.float32), preferred_element_type=jnp.float32))
    restored = jnp.dot(left_old.astype(jnp.float32), moment.astype(jnp.float32), preferred_element_type=jnp.float32).astype(jnp.bfloat16)
    mixed = (moment_decay * jnp.dot(restored.astype(jnp.float32), right_old.T.astype(jnp.float32), preferred_element_type=jnp.float32) + (1.0 - moment_decay) * gradient.astype(jnp.float32)).astype(jnp.bfloat16)
    turned = jnp.dot(left_basis.T.astype(jnp.float32), mixed.astype(jnp.float32), preferred_element_type=jnp.float32).astype(jnp.bfloat16)
    moment_new = jnp.dot(turned.astype(jnp.float32), right_basis.astype(jnp.float32), preferred_element_type=jnp.float32).astype(jnp.bfloat16)
    return (left_stat, right_statistic, left_basis, right_basis, moment_new)

def reference(grad_part, owner, moment, gram_left, gram_right, basis_left, basis_right):
    total = jnp.zeros(grad_part.shape[1:], jnp.float32)
    for replica in range(N_DP):
        total = total + grad_part[replica].astype(jnp.float32)
    gradient = total.astype(jnp.bfloat16)
    numbers = jax.vmap(slot_numbers)(owner).reshape(-1).astype(jnp.int32)
    owners_flat = owner.reshape(-1).astype(jnp.int32)
    groups = (jnp.arange(NB) // BLOCKS_PER_GROUP).astype(jnp.int32)

    def one_block(block_index):
        group_at = groups[block_index]
        owner_at = owners_flat[block_index]
        slot_at = numbers[block_index]
        return refresh(gram_left[group_at, owner_at, slot_at], gram_right[group_at, owner_at, slot_at], basis_left[group_at, owner_at, slot_at], basis_right[group_at, owner_at, slot_at], gradient[block_index], moment[block_index])
    results = lax.map(one_block, jnp.arange(NB).astype(jnp.int32))
    placed = []
    for which in range(4):
        placed.append(jnp.zeros(gram_left.shape, jnp.bfloat16).at[groups, owners_flat, numbers].set(results[which]))
    return (placed[0], placed[1], placed[2], placed[3], results[4])
```

```python
import functools

import jax
import jax.numpy as jnp
from jax import lax
from jax.experimental import pallas as pl
from jax.experimental.pallas import tpu as pltpu
from jax.sharding import PartitionSpec as P

gram_decay = 0.85
moment_decay = 0.9


def slot_numbers(row):
    length = row.shape[0]
    equal_owner = row[:, None] == row[None, :]
    earlier = lax.broadcasted_iota(jnp.int32, (length, length), 1) < lax.broadcasted_iota(
        jnp.int32, (length, length), 0
    )
    return jnp.sum(jnp.where(equal_owner & earlier, 1, 0), axis=1).astype(jnp.int32)


def slot_mapping(row, slot_count, owner_count):
    numbers = slot_numbers(row)
    by_owner = row[:, None, None] == lax.broadcasted_iota(jnp.int32, (1, 1, owner_count), 2)
    by_slot = numbers[:, None, None] == lax.broadcasted_iota(jnp.int32, (1, slot_count, 1), 1)
    return (by_owner & by_slot).astype(jnp.bfloat16)


def pack_rows(onehot, rows_in):
    spread = jnp.einsum("jso,jrc->sorc", onehot, rows_in, preferred_element_type=jnp.float32)
    return spread.astype(jnp.bfloat16).reshape(
        spread.shape[0], spread.shape[1] * spread.shape[2], spread.shape[3]
    )


HI = lax.Precision.HIGHEST

def _nt(a, b):
    return lax.dot_general(a, b, (((1,), (1,)), ((), ())), precision=HI,
                           preferred_element_type=jnp.float32)

def _orth_kernel(s_ref, p_ref, q_ref, a_ref, m_ref, w_ref, qf_ref, *, nb):
    bsz, n, _ = s_ref.shape
    kb = n // nb
    a_ref[...] = s_ref[...]
    eye = (lax.broadcasted_iota(jnp.int32, (nb, nb), 0)
           == lax.broadcasted_iota(jnp.int32, (nb, nb), 1)).astype(jnp.float32)
    lane = lax.broadcasted_iota(jnp.int32, (1, 1, 2 * nb), 2)
    lane_l = lax.broadcasted_iota(jnp.int32, (1, 1, nb), 2)
    sub = lax.broadcasted_iota(jnp.int32, (1, nb, 1), 1)
    for k in range(kb):
        k0 = k * nb
        m_ref[:, :, :nb] = a_ref[:, k0:k0 + nb, k0:k0 + nb]
        m_ref[:, :, nb:] = jnp.broadcast_to(eye, (bsz, nb, nb))

        def step(j, carry):
            row = m_ref[:, pl.ds(j, 1), :]
            piv = jnp.sum(jnp.where(lane == j, row, 0.0), axis=-1, keepdims=True)
            inv_s = 1.0 / jnp.sqrt(piv)
            scaled = row * inv_s
            left = m_ref[:, :, :nb]
            col = jnp.sum(jnp.where(lane_l == j, left, 0.0), axis=-1, keepdims=True) * inv_s
            col = jnp.where(sub > j, col, 0.0)
            m_ref[...] = m_ref[...] - col * scaled
            m_ref[:, pl.ds(j, 1), :] = scaled
            return carry

        lax.fori_loop(0, nb, step, 0)
        w_ref[:, k] = m_ref[:, :, nb:]
        if k < kb - 1:
            for b in range(bsz):
                panel = _nt(a_ref[b, k0 + nb:, k0:k0 + nb], w_ref[b, k])
                a_ref[b, k0 + nb:, k0:k0 + nb] = panel
                a_ref[b, k0 + nb:, k0 + nb:] = a_ref[b, k0 + nb:, k0 + nb:] - _nt(panel, panel)
    for k in range(kb):
        k0 = k * nb
        for b in range(bsz):
            rhs = p_ref[b, :, k0:k0 + nb]
            if k > 0:
                rhs = rhs - _nt(qf_ref[b, :, :k0], a_ref[b, k0:k0 + nb, :k0])
            qf_ref[b, :, k0:k0 + nb] = _nt(rhs, w_ref[b, k])
    q_ref[...] = qf_ref[...].astype(q_ref.dtype)


def orth_batch(square, power, nb=128):
    bsz, n, _ = square.shape
    vmem = pltpu.VMEM
    return pl.pallas_call(
        functools.partial(_orth_kernel, nb=nb),
        out_shape=jax.ShapeDtypeStruct((bsz, n, n), jnp.bfloat16),
        in_specs=[pl.BlockSpec(memory_space=vmem)] * 2,
        out_specs=pl.BlockSpec(memory_space=vmem),
        scratch_shapes=[
            vmem((bsz, n, n), jnp.float32),
            vmem((bsz, nb, 2 * nb), jnp.float32),
            vmem((bsz, n // nb, nb, nb), jnp.float32),
            vmem((bsz, n, n), jnp.float32),
        ],
        compiler_params=pltpu.CompilerParams(vmem_limit_bytes=60 * 1024 * 1024),
    )(square, power)


def refresh_all(left_gram, right_gram, left_old, right_old, gradient, moment):
    block_width = gradient.shape[-1]
    slots = gradient.shape[0]
    outer_left = jnp.einsum("sij,skj->sik", gradient, gradient, preferred_element_type=jnp.float32)
    outer_right = jnp.einsum("sji,sjk->sik", gradient, gradient, preferred_element_type=jnp.float32)
    left_stat = (
        gram_decay * left_gram.astype(jnp.float32) + (1.0 - gram_decay) / block_width * outer_left
    ).astype(jnp.bfloat16)
    right_statistic = (
        gram_decay * right_gram.astype(jnp.float32) + (1.0 - gram_decay) / block_width * outer_right
    ).astype(jnp.bfloat16)
    left_power = jnp.einsum("sij,sjk->sik", left_stat, left_old, preferred_element_type=jnp.float32)
    right_power = jnp.einsum(
        "sij,sjk->sik", right_statistic, right_old, preferred_element_type=jnp.float32
    )
    power = jnp.concatenate([left_power, right_power], axis=0)
    square = jnp.einsum(
        "bji,bjk->bik", power, power, precision=lax.Precision.HIGHEST,
        preferred_element_type=jnp.float32,
    )
    basis = orth_batch(square, power)
    left_basis, right_basis = basis[:slots], basis[slots:]
    restored = jnp.einsum(
        "sij,sjk->sik", left_old, moment, preferred_element_type=jnp.float32
    ).astype(jnp.bfloat16)
    mixed = (
        moment_decay
        * jnp.einsum("sij,skj->sik", restored, right_old, preferred_element_type=jnp.float32)
        + (1.0 - moment_decay) * gradient.astype(jnp.float32)
    ).astype(jnp.bfloat16)
    turned = jnp.einsum(
        "sji,sjk->sik", left_basis, mixed, preferred_element_type=jnp.float32
    ).astype(jnp.bfloat16)
    moment_new = jnp.einsum(
        "sij,sjk->sik", turned, right_basis, preferred_element_type=jnp.float32
    ).astype(jnp.bfloat16)
    return (left_stat, right_statistic, left_basis, right_basis, moment_new)


def local(grad_part, owner, moment, gram_left, gram_right, basis_left, basis_right):
    owner_count = lax.axis_size("mp")
    my_index = lax.axis_index("mp")
    my_group = lax.axis_index("dp")
    row_count = moment.shape[1]
    block_width = moment.shape[2]
    slot_count = gram_left.shape[2]
    my_table = lax.dynamic_index_in_dim(owner, my_group, 0, keepdims=False)
    onehot = slot_mapping(my_table, slot_count, owner_count)
    summed = lax.psum_scatter(
        grad_part[0].astype(jnp.float32).astype(jnp.bfloat16), "dp", scatter_dimension=0, tiled=True
    )
    grads, moments = (
        lax.all_to_all(pack_rows(onehot, summed), "mp", split_axis=1, concat_axis=1, tiled=True),
        lax.all_to_all(pack_rows(onehot, moment), "mp", split_axis=1, concat_axis=1, tiled=True),
    )
    my_load = jnp.sum(jnp.where(my_table == my_index, 1, 0))
    results = refresh_all(
        gram_left[0, 0], gram_right[0, 0], basis_left[0, 0], basis_right[0, 0], grads, moments
    )
    live = (lax.broadcasted_iota(jnp.int32, (slot_count, 1, 1), 0) < my_load)
    results = [jnp.where(live, r, jnp.zeros_like(r)) for r in results]
    stacked = [results[which][None, None] for which in range(4)]
    turned_back = results[4]
    landed = lax.all_to_all(turned_back, "mp", split_axis=1, concat_axis=1, tiled=True)
    landed = landed.reshape(slot_count, owner_count, row_count, block_width)
    moment_new = jnp.einsum(
        "jso,sorc->jrc", onehot, landed, preferred_element_type=jnp.float32
    ).astype(jnp.bfloat16)
    return (stacked[0], stacked[1], stacked[2], stacked[3], moment_new)


def solution(mesh):
    return jax.shard_map(
        local,
        mesh=mesh,
        in_specs=(
            P("dp", None, "mp", None),
            P(),
            P("dp", "mp", None),
            P("dp", "mp", None, None, None),
            P("dp", "mp", None, None, None),
            P("dp", "mp", None, None, None),
            P("dp", "mp", None, None, None),
        ),
        out_specs=(
            P("dp", "mp", None, None, None),
            P("dp", "mp", None, None, None),
            P("dp", "mp", None, None, None),
            P("dp", "mp", None, None, None),
            P("dp", "mp", None),
        ),
        check_vma=False,
    )
```

```python
import functools

import jax
import jax.numpy as jnp
from jax import lax
from jax.experimental import pallas as pl
from jax.experimental.pallas import tpu as pltpu
from jax.sharding import PartitionSpec as P

gram_decay = 0.85
moment_decay = 0.9


def slot_numbers(row):
    length = row.shape[0]
    equal_owner = row[:, None] == row[None, :]
    earlier = lax.broadcasted_iota(jnp.int32, (length, length), 1) < lax.broadcasted_iota(
        jnp.int32, (length, length), 0
    )
    return jnp.sum(jnp.where(equal_owner & earlier, 1, 0), axis=1).astype(jnp.int32)


def slot_mapping(row, slot_count, owner_count):
    numbers = slot_numbers(row)
    by_owner = row[:, None, None] == lax.broadcasted_iota(jnp.int32, (1, 1, owner_count), 2)
    by_slot = numbers[:, None, None] == lax.broadcasted_iota(jnp.int32, (1, slot_count, 1), 1)
    return (by_owner & by_slot).astype(jnp.bfloat16)


def pack_rows(onehot, rows_in):
    spread = jnp.einsum("jso,jrc->sorc", onehot, rows_in, preferred_element_type=jnp.float32)
    return spread.astype(jnp.bfloat16).reshape(
        spread.shape[0], spread.shape[1] * spread.shape[2], spread.shape[3]
    )


HI = lax.Precision.HIGHEST

def _nt(a, b):
    return lax.dot_general(a, b, (((1,), (1,)), ((), ())), precision=HI,
                           preferred_element_type=jnp.float32)

def _orth_kernel(s_ref, p_ref, q_ref, a_ref, m_ref, w_ref, qf_ref, *, nb):
    bsz, n, _ = s_ref.shape
    kb = n // nb
    a_ref[...] = s_ref[...]
    lane_l = lax.broadcasted_iota(jnp.int32, (1, 1, nb), 2)
    for k in range(kb):
        k0 = k * nb
        m_ref[...] = a_ref[:, k0:k0 + nb, k0:k0 + nb]
        for t in range(nb // 8):
            r0 = 8 * t
            sub = lax.broadcasted_iota(jnp.int32, (1, nb - r0, 1), 1) + r0

            def step(jj, carry, r0=r0, sub=sub):
                j = r0 + jj
                row = m_ref[:, pl.ds(j, 1), :]
                at_j = lane_l == j
                piv = jnp.sum(jnp.where(at_j, row, 0.0), axis=-1, keepdims=True)
                inv_s = 1.0 / jnp.sqrt(piv)
                scaled = jnp.where(at_j, inv_s, row * inv_s)
                blk = m_ref[:, r0:, :]
                below = sub > j
                col = jnp.sum(jnp.where(at_j, blk, 0.0), axis=-1, keepdims=True) * inv_s
                col = jnp.where(below, col, 0.0)
                blk = jnp.where(at_j & below, 0.0, blk) - col * scaled
                m_ref[:, r0:, :] = blk
                m_ref[:, pl.ds(j, 1), :] = scaled
                return carry

            lax.fori_loop(0, 8, step, 0, unroll=True)
        low = (lax.broadcasted_iota(jnp.int32, (1, nb, nb), 2)
               <= lax.broadcasted_iota(jnp.int32, (1, nb, nb), 1))
        w_ref[:, k] = jnp.where(low, m_ref[...], 0.0)
        if k < kb - 1:
            for b in range(bsz):
                panel = _nt(a_ref[b, k0 + nb:, k0:k0 + nb], w_ref[b, k])
                a_ref[b, k0 + nb:, k0:k0 + nb] = panel
                a_ref[b, k0 + nb:, k0 + nb:] = a_ref[b, k0 + nb:, k0 + nb:] - _nt(panel, panel)
    for k in range(kb):
        k0 = k * nb
        for b in range(bsz):
            rhs = p_ref[b, :, k0:k0 + nb]
            if k > 0:
                rhs = rhs - _nt(qf_ref[b, :, :k0], a_ref[b, k0:k0 + nb, :k0])
            qf_ref[b, :, k0:k0 + nb] = _nt(rhs, w_ref[b, k])
    q_ref[...] = qf_ref[...].astype(q_ref.dtype)


def orth_batch(square, power, nb=128):
    bsz, n, _ = square.shape
    vmem = pltpu.VMEM
    return pl.pallas_call(
        functools.partial(_orth_kernel, nb=nb),
        out_shape=jax.ShapeDtypeStruct((bsz, n, n), jnp.bfloat16),
        in_specs=[pl.BlockSpec(memory_space=vmem)] * 2,
        out_specs=pl.BlockSpec(memory_space=vmem),
        scratch_shapes=[
            vmem((bsz, n, n), jnp.float32),
            vmem((bsz, nb, nb), jnp.float32),
            vmem((bsz, n // nb, nb, nb), jnp.float32),
            vmem((bsz, n, n), jnp.float32),
        ],
        compiler_params=pltpu.CompilerParams(vmem_limit_bytes=60 * 1024 * 1024),
    )(square, power)


def refresh_all(left_gram, right_gram, left_old, right_old, gradient, moment):
    block_width = gradient.shape[-1]
    slots = gradient.shape[0]
    outer_left = jnp.einsum("sij,skj->sik", gradient, gradient, preferred_element_type=jnp.float32)
    outer_right = jnp.einsum("sji,sjk->sik", gradient, gradient, preferred_element_type=jnp.float32)
    left_stat = (
        gram_decay * left_gram.astype(jnp.float32) + (1.0 - gram_decay) / block_width * outer_left
    ).astype(jnp.bfloat16)
    right_statistic = (
        gram_decay * right_gram.astype(jnp.float32) + (1.0 - gram_decay) / block_width * outer_right
    ).astype(jnp.bfloat16)
    left_power = jnp.einsum("sij,sjk->sik", left_stat, left_old, preferred_element_type=jnp.float32)
    right_power = jnp.einsum(
        "sij,sjk->sik", right_statistic, right_old, preferred_element_type=jnp.float32
    )
    power = jnp.concatenate([left_power, right_power], axis=0)
    square = jnp.einsum(
        "bji,bjk->bik", power, power, precision=lax.Precision.HIGHEST,
        preferred_element_type=jnp.float32,
    )
    basis = orth_batch(square, power)
    left_basis, right_basis = basis[:slots], basis[slots:]
    restored = jnp.einsum(
        "sij,sjk->sik", left_old, moment, preferred_element_type=jnp.float32
    ).astype(jnp.bfloat16)
    mixed = (
        moment_decay
        * jnp.einsum("sij,skj->sik", restored, right_old, preferred_element_type=jnp.float32)
        + (1.0 - moment_decay) * gradient.astype(jnp.float32)
    ).astype(jnp.bfloat16)
    turned = jnp.einsum(
        "sji,sjk->sik", left_basis, mixed, preferred_element_type=jnp.float32
    ).astype(jnp.bfloat16)
    moment_new = jnp.einsum(
        "sij,sjk->sik", turned, right_basis, preferred_element_type=jnp.float32
    ).astype(jnp.bfloat16)
    return (left_stat, right_statistic, left_basis, right_basis, moment_new)


def local(grad_part, owner, moment, gram_left, gram_right, basis_left, basis_right):
    owner_count = lax.axis_size("mp")
    my_index = lax.axis_index("mp")
    my_group = lax.axis_index("dp")
    row_count = moment.shape[1]
    block_width = moment.shape[2]
    slot_count = gram_left.shape[2]
    my_table = lax.dynamic_index_in_dim(owner, my_group, 0, keepdims=False)
    onehot = slot_mapping(my_table, slot_count, owner_count)
    summed = lax.psum_scatter(
        grad_part[0].astype(jnp.float32).astype(jnp.bfloat16), "dp", scatter_dimension=0, tiled=True
    )
    grads, moments = (
        lax.all_to_all(pack_rows(onehot, summed), "mp", split_axis=1, concat_axis=1, tiled=True),
        lax.all_to_all(pack_rows(onehot, moment), "mp", split_axis=1, concat_axis=1, tiled=True),
    )
    my_load = jnp.sum(jnp.where(my_table == my_index, 1, 0))
    results = refresh_all(
        gram_left[0, 0], gram_right[0, 0], basis_left[0, 0], basis_right[0, 0], grads, moments
    )
    live = (lax.broadcasted_iota(jnp.int32, (slot_count, 1, 1), 0) < my_load)
    results = [jnp.where(live, r, jnp.zeros_like(r)) for r in results]
    stacked = [results[which][None, None] for which in range(4)]
    turned_back = results[4]
    landed = lax.all_to_all(turned_back, "mp", split_axis=1, concat_axis=1, tiled=True)
    landed = landed.reshape(slot_count, owner_count, row_count, block_width)
    moment_new = jnp.einsum(
        "jso,sorc->jrc", onehot, landed, preferred_element_type=jnp.float32
    ).astype(jnp.bfloat16)
    return (stacked[0], stacked[1], stacked[2], stacked[3], moment_new)


def solution(mesh):
    return jax.shard_map(
        local,
        mesh=mesh,
        in_specs=(
            P("dp", None, "mp", None),
            P(),
            P("dp", "mp", None),
            P("dp", "mp", None, None, None),
            P("dp", "mp", None, None, None),
            P("dp", "mp", None, None, None),
            P("dp", "mp", None, None, None),
        ),
        out_specs=(
            P("dp", "mp", None, None, None),
            P("dp", "mp", None, None, None),
            P("dp", "mp", None, None, None),
            P("dp", "mp", None, None, None),
            P("dp", "mp", None),
        ),
        check_vma=False,
    )
```

```python
import functools

import jax
import jax.numpy as jnp
from jax import lax
from jax.experimental import pallas as pl
from jax.experimental.pallas import tpu as pltpu
from jax.sharding import PartitionSpec as P

gram_decay = 0.85
moment_decay = 0.9


def slot_numbers(row):
    length = row.shape[0]
    equal_owner = row[:, None] == row[None, :]
    earlier = lax.broadcasted_iota(jnp.int32, (length, length), 1) < lax.broadcasted_iota(
        jnp.int32, (length, length), 0
    )
    return jnp.sum(jnp.where(equal_owner & earlier, 1, 0), axis=1).astype(jnp.int32)


def slot_mapping(row, slot_count, owner_count):
    numbers = slot_numbers(row)
    by_owner = row[:, None, None] == lax.broadcasted_iota(jnp.int32, (1, 1, owner_count), 2)
    by_slot = numbers[:, None, None] == lax.broadcasted_iota(jnp.int32, (1, slot_count, 1), 1)
    return (by_owner & by_slot).astype(jnp.bfloat16)


def pack_rows(onehot, rows_in):
    spread = jnp.einsum("jso,jrc->sorc", onehot, rows_in, preferred_element_type=jnp.float32)
    return spread.astype(jnp.bfloat16).reshape(
        spread.shape[0], spread.shape[1] * spread.shape[2], spread.shape[3]
    )


HI = lax.Precision.HIGHEST

def _nt(a, b):
    return lax.dot_general(a, b, (((1,), (1,)), ((), ())), precision=HI,
                           preferred_element_type=jnp.float32)

def _orth_kernel(s_ref, p_ref, q_ref, a_ref, m_ref, w_ref, qf_ref, *, nb):
    bsz, n, _ = s_ref.shape
    kb = n // nb
    a_ref[...] = s_ref[...]
    lane_l = lax.broadcasted_iota(jnp.int32, (1, 1, nb), 2)
    for k in range(kb):
        k0 = k * nb
        m_ref[...] = a_ref[:, k0:k0 + nb, k0:k0 + nb]
        for t in range(nb // 8):
            r0 = 8 * t
            sub = lax.broadcasted_iota(jnp.int32, (1, nb - r0, 1), 1) + r0

            def step(jj, carry, r0=r0, sub=sub):
                j = r0 + jj
                row = m_ref[:, pl.ds(j, 1), :]
                at_j = lane_l == j
                piv = jnp.sum(jnp.where(at_j, row, 0.0), axis=-1, keepdims=True)
                inv_s = lax.rsqrt(piv)
                scaled = jnp.where(at_j, inv_s, row * inv_s)
                blk = m_ref[:, r0:, :]
                below = sub > j
                col = jnp.sum(jnp.where(at_j, blk, 0.0), axis=-1, keepdims=True) * inv_s
                col = jnp.where(below, col, 0.0)
                blk = jnp.where(at_j & below, 0.0, blk) - col * scaled
                m_ref[:, r0:, :] = blk
                m_ref[:, pl.ds(j, 1), :] = scaled
                return carry

            lax.fori_loop(0, 8, step, 0, unroll=True)
        low = (lax.broadcasted_iota(jnp.int32, (1, nb, nb), 2)
               <= lax.broadcasted_iota(jnp.int32, (1, nb, nb), 1))
        w_ref[:, k] = jnp.where(low, m_ref[...], 0.0)
        if k < kb - 1:
            for b in range(bsz):
                panel = _nt(a_ref[b, k0 + nb:, k0:k0 + nb], w_ref[b, k])
                a_ref[b, k0 + nb:, k0:k0 + nb] = panel
                a_ref[b, k0 + nb:, k0 + nb:] = a_ref[b, k0 + nb:, k0 + nb:] - _nt(panel, panel)
    for k in range(kb):
        k0 = k * nb
        for b in range(bsz):
            rhs = p_ref[b, :, k0:k0 + nb]
            if k > 0:
                rhs = rhs - _nt(qf_ref[b, :, :k0], a_ref[b, k0:k0 + nb, :k0])
            qf_ref[b, :, k0:k0 + nb] = _nt(rhs, w_ref[b, k])
    q_ref[...] = qf_ref[...].astype(q_ref.dtype)


def orth_batch(square, power, nb=128):
    bsz, n, _ = square.shape
    vmem = pltpu.VMEM
    return pl.pallas_call(
        functools.partial(_orth_kernel, nb=nb),
        out_shape=jax.ShapeDtypeStruct((bsz, n, n), jnp.bfloat16),
        in_specs=[pl.BlockSpec(memory_space=vmem)] * 2,
        out_specs=pl.BlockSpec(memory_space=vmem),
        scratch_shapes=[
            vmem((bsz, n, n), jnp.float32),
            vmem((bsz, nb, nb), jnp.float32),
            vmem((bsz, n // nb, nb, nb), jnp.float32),
            vmem((bsz, n, n), jnp.float32),
        ],
        compiler_params=pltpu.CompilerParams(vmem_limit_bytes=60 * 1024 * 1024),
    )(square, power)


def refresh_all(left_gram, right_gram, left_old, right_old, gradient, moment):
    block_width = gradient.shape[-1]
    slots = gradient.shape[0]
    outer_left = jnp.einsum("sij,skj->sik", gradient, gradient, preferred_element_type=jnp.float32)
    outer_right = jnp.einsum("sji,sjk->sik", gradient, gradient, preferred_element_type=jnp.float32)
    left_stat = (
        gram_decay * left_gram.astype(jnp.float32) + (1.0 - gram_decay) / block_width * outer_left
    ).astype(jnp.bfloat16)
    right_statistic = (
        gram_decay * right_gram.astype(jnp.float32) + (1.0 - gram_decay) / block_width * outer_right
    ).astype(jnp.bfloat16)
    left_power = jnp.einsum("sij,sjk->sik", left_stat, left_old, preferred_element_type=jnp.float32)
    right_power = jnp.einsum(
        "sij,sjk->sik", right_statistic, right_old, preferred_element_type=jnp.float32
    )
    power = jnp.concatenate([left_power, right_power], axis=0)
    square = jnp.einsum(
        "bji,bjk->bik", power, power, precision=lax.Precision.HIGHEST,
        preferred_element_type=jnp.float32,
    )
    basis = orth_batch(square, power)
    left_basis, right_basis = basis[:slots], basis[slots:]
    restored = jnp.einsum(
        "sij,sjk->sik", left_old, moment, preferred_element_type=jnp.float32
    ).astype(jnp.bfloat16)
    mixed = (
        moment_decay
        * jnp.einsum("sij,skj->sik", restored, right_old, preferred_element_type=jnp.float32)
        + (1.0 - moment_decay) * gradient.astype(jnp.float32)
    ).astype(jnp.bfloat16)
    turned = jnp.einsum(
        "sji,sjk->sik", left_basis, mixed, preferred_element_type=jnp.float32
    ).astype(jnp.bfloat16)
    moment_new = jnp.einsum(
        "sij,sjk->sik", turned, right_basis, preferred_element_type=jnp.float32
    ).astype(jnp.bfloat16)
    return (left_stat, right_statistic, left_basis, right_basis, moment_new)


def local(grad_part, owner, moment, gram_left, gram_right, basis_left, basis_right):
    owner_count = lax.axis_size("mp")
    my_index = lax.axis_index("mp")
    my_group = lax.axis_index("dp")
    row_count = moment.shape[1]
    block_width = moment.shape[2]
    slot_count = gram_left.shape[2]
    my_table = lax.dynamic_index_in_dim(owner, my_group, 0, keepdims=False)
    onehot = slot_mapping(my_table, slot_count, owner_count)
    replica_count = lax.axis_size("dp")
    parts = lax.all_to_all(grad_part[0], "dp", split_axis=0, concat_axis=0, tiled=True)
    parts = parts.reshape((replica_count, -1) + parts.shape[1:])
    total = jnp.zeros(parts.shape[1:], jnp.float32)
    for replica in range(replica_count):
        total = total + parts[replica].astype(jnp.float32)
    summed = total.astype(jnp.bfloat16)
    grads, moments = (
        lax.all_to_all(pack_rows(onehot, summed), "mp", split_axis=1, concat_axis=1, tiled=True),
        lax.all_to_all(pack_rows(onehot, moment), "mp", split_axis=1, concat_axis=1, tiled=True),
    )
    my_load = jnp.sum(jnp.where(my_table == my_index, 1, 0))
    results = refresh_all(
        gram_left[0, 0], gram_right[0, 0], basis_left[0, 0], basis_right[0, 0], grads, moments
    )
    live = (lax.broadcasted_iota(jnp.int32, (slot_count, 1, 1), 0) < my_load)
    results = [jnp.where(live, r, jnp.zeros_like(r)) for r in results]
    stacked = [results[which][None, None] for which in range(4)]
    turned_back = results[4]
    landed = lax.all_to_all(turned_back, "mp", split_axis=1, concat_axis=1, tiled=True)
    landed = landed.reshape(slot_count, owner_count, row_count, block_width)
    moment_new = jnp.einsum(
        "jso,sorc->jrc", onehot, landed, preferred_element_type=jnp.float32
    ).astype(jnp.bfloat16)
    return (stacked[0], stacked[1], stacked[2], stacked[3], moment_new)


def solution(mesh):
    return jax.shard_map(
        local,
        mesh=mesh,
        in_specs=(
            P("dp", None, "mp", None),
            P(),
            P("dp", "mp", None),
            P("dp", "mp", None, None, None),
            P("dp", "mp", None, None, None),
            P("dp", "mp", None, None, None),
            P("dp", "mp", None, None, None),
        ),
        out_specs=(
            P("dp", "mp", None, None, None),
            P("dp", "mp", None, None, None),
            P("dp", "mp", None, None, None),
            P("dp", "mp", None, None, None),
            P("dp", "mp", None),
        ),
        check_vma=False,
    )
```

```python
import functools

import jax
import jax.numpy as jnp
from jax import lax
from jax.experimental import pallas as pl
from jax.experimental.pallas import tpu as pltpu
from jax.sharding import PartitionSpec as P

gram_decay = 0.85
moment_decay = 0.9


def slot_numbers(row):
    length = row.shape[0]
    equal_owner = row[:, None] == row[None, :]
    earlier = lax.broadcasted_iota(jnp.int32, (length, length), 1) < lax.broadcasted_iota(
        jnp.int32, (length, length), 0
    )
    return jnp.sum(jnp.where(equal_owner & earlier, 1, 0), axis=1).astype(jnp.int32)


def slot_mapping(row, slot_count, owner_count):
    numbers = slot_numbers(row)
    by_owner = row[:, None, None] == lax.broadcasted_iota(jnp.int32, (1, 1, owner_count), 2)
    by_slot = numbers[:, None, None] == lax.broadcasted_iota(jnp.int32, (1, slot_count, 1), 1)
    return (by_owner & by_slot).astype(jnp.bfloat16)


def pack_rows(onehot, rows_in):
    spread = jnp.einsum("jso,jrc->sorc", onehot, rows_in, preferred_element_type=jnp.float32)
    return spread.astype(jnp.bfloat16).reshape(
        spread.shape[0], spread.shape[1] * spread.shape[2], spread.shape[3]
    )


HI = lax.Precision.HIGHEST

def _nt(a, b):
    return lax.dot_general(a, b, (((1,), (1,)), ((), ())), precision=HI,
                           preferred_element_type=jnp.float32)

def _orth_kernel(s_ref, p_ref, q_ref, a_ref, m_ref, w_ref, qf_ref, *, nb):
    bsz, n, _ = s_ref.shape
    kb = n // nb
    a_ref[...] = s_ref[...]
    lane_l = lax.broadcasted_iota(jnp.int32, (1, 1, nb), 2)
    for k in range(kb):
        k0 = k * nb
        m_ref[...] = a_ref[:, k0:k0 + nb, k0:k0 + nb]
        for t in range(nb // 8):
            r0 = 8 * t
            sub = lax.broadcasted_iota(jnp.int32, (1, nb - r0, 1), 1) + r0

            def step(jj, carry, r0=r0, sub=sub):
                j = r0 + jj
                row = m_ref[:, pl.ds(j, 1), :]
                at_j = lane_l == j
                piv = jnp.sum(jnp.where(at_j, row, 0.0), axis=-1, keepdims=True)
                inv_s = lax.rsqrt(piv)
                scaled = jnp.where(at_j, inv_s, row * inv_s)
                blk = m_ref[:, r0:, :]
                below = sub > j
                col = jnp.sum(jnp.where(at_j, blk, 0.0), axis=-1, keepdims=True) * inv_s
                col = jnp.where(below, col, 0.0)
                blk = jnp.where(at_j & below, 0.0, blk) - col * scaled
                m_ref[:, r0:, :] = blk
                m_ref[:, pl.ds(j, 1), :] = scaled
                return carry

            lax.fori_loop(0, 8, step, 0, unroll=True)
        low = (lax.broadcasted_iota(jnp.int32, (1, nb, nb), 2)
               <= lax.broadcasted_iota(jnp.int32, (1, nb, nb), 1))
        w_ref[:, k] = jnp.where(low, m_ref[...], 0.0)
        if k < kb - 1:
            for b in range(bsz):
                panel = _nt(a_ref[b, k0 + nb:, k0:k0 + nb], w_ref[b, k])
                a_ref[b, k0 + nb:, k0:k0 + nb] = panel
                a_ref[b, k0 + nb:, k0 + nb:] = a_ref[b, k0 + nb:, k0 + nb:] - _nt(panel, panel)
    for k in range(kb):
        k0 = k * nb
        for b in range(bsz):
            rhs = p_ref[b, :, k0:k0 + nb]
            if k > 0:
                rhs = rhs - _nt(qf_ref[b, :, :k0], a_ref[b, k0:k0 + nb, :k0])
            qf_ref[b, :, k0:k0 + nb] = _nt(rhs, w_ref[b, k])
    q_ref[...] = qf_ref[...].astype(q_ref.dtype)


def orth_batch(square, power, nb=128):
    bsz, n, _ = square.shape
    vmem = pltpu.VMEM
    return pl.pallas_call(
        functools.partial(_orth_kernel, nb=nb),
        out_shape=jax.ShapeDtypeStruct((bsz, n, n), jnp.bfloat16),
        in_specs=[pl.BlockSpec(memory_space=vmem)] * 2,
        out_specs=pl.BlockSpec(memory_space=vmem),
        scratch_shapes=[
            vmem((bsz, n, n), jnp.float32),
            vmem((bsz, nb, nb), jnp.float32),
            vmem((bsz, n // nb, nb, nb), jnp.float32),
            vmem((bsz, n, n), jnp.float32),
        ],
        compiler_params=pltpu.CompilerParams(vmem_limit_bytes=60 * 1024 * 1024),
    )(square, power)


def refresh_all(left_gram, right_gram, left_old, right_old, gradient, moment):
    block_width = gradient.shape[-1]
    slots = gradient.shape[0]
    outer_left = jnp.einsum("sij,skj->sik", gradient, gradient, preferred_element_type=jnp.float32)
    outer_right = jnp.einsum("sji,sjk->sik", gradient, gradient, preferred_element_type=jnp.float32)
    left_stat = (
        gram_decay * left_gram.astype(jnp.float32) + (1.0 - gram_decay) / block_width * outer_left
    ).astype(jnp.bfloat16)
    right_statistic = (
        gram_decay * right_gram.astype(jnp.float32) + (1.0 - gram_decay) / block_width * outer_right
    ).astype(jnp.bfloat16)
    left_power = jnp.einsum("sij,sjk->sik", left_stat, left_old, preferred_element_type=jnp.float32)
    right_power = jnp.einsum(
        "sij,sjk->sik", right_statistic, right_old, preferred_element_type=jnp.float32
    )
    power = jnp.concatenate([left_power, right_power], axis=0)
    square = jnp.einsum(
        "bji,bjk->bik", power, power, precision=lax.Precision.HIGHEST,
        preferred_element_type=jnp.float32,
    )
    basis = orth_batch(square, power)
    left_basis, right_basis = basis[:slots], basis[slots:]
    restored = jnp.einsum(
        "sij,sjk->sik", left_old, moment, preferred_element_type=jnp.float32
    ).astype(jnp.bfloat16)
    mixed = (
        moment_decay
        * jnp.einsum("sij,skj->sik", restored, right_old, preferred_element_type=jnp.float32)
        + (1.0 - moment_decay) * gradient.astype(jnp.float32)
    ).astype(jnp.bfloat16)
    turned = jnp.einsum(
        "sji,sjk->sik", left_basis, mixed, preferred_element_type=jnp.float32
    ).astype(jnp.bfloat16)
    moment_new = jnp.einsum(
        "sij,sjk->sik", turned, right_basis, preferred_element_type=jnp.float32
    ).astype(jnp.bfloat16)
    return (left_stat, right_statistic, left_basis, right_basis, moment_new)


def local(grad_part, owner, moment, gram_left, gram_right, basis_left, basis_right):
    owner_count = lax.axis_size("mp")
    my_index = lax.axis_index("mp")
    my_group = lax.axis_index(("dpo", "dpi"))
    row_count = moment.shape[1]
    block_width = moment.shape[2]
    slot_count = gram_left.shape[2]
    my_table = lax.dynamic_index_in_dim(owner, my_group, 0, keepdims=False)
    onehot = slot_mapping(my_table, slot_count, owner_count)
    outer_count, inner_count = lax.axis_size("dpo"), lax.axis_size("dpi")
    parts = grad_part[0].reshape((outer_count, inner_count, -1) + grad_part.shape[2:])
    parts = lax.all_to_all(parts, "dpi", split_axis=1, concat_axis=1, tiled=True)
    half = jnp.zeros(parts.shape[:1] + parts.shape[2:], jnp.float32)
    for source in range(inner_count):
        half = half + parts[:, source].astype(jnp.float32)
    parts = lax.all_to_all(half.astype(jnp.bfloat16), "dpo", split_axis=0, concat_axis=0, tiled=True)
    total = jnp.zeros(parts.shape[1:], jnp.float32)
    for source in range(outer_count):
        total = total + parts[source].astype(jnp.float32)
    summed = total.astype(jnp.bfloat16)
    grads, moments = (
        lax.all_to_all(pack_rows(onehot, summed), "mp", split_axis=1, concat_axis=1, tiled=True),
        lax.all_to_all(pack_rows(onehot, moment), "mp", split_axis=1, concat_axis=1, tiled=True),
    )
    my_load = jnp.sum(jnp.where(my_table == my_index, 1, 0))
    results = refresh_all(
        gram_left[0, 0], gram_right[0, 0], basis_left[0, 0], basis_right[0, 0], grads, moments
    )
    live = (lax.broadcasted_iota(jnp.int32, (slot_count, 1, 1), 0) < my_load)
    results = [jnp.where(live, r, jnp.zeros_like(r)) for r in results]
    stacked = [results[which][None, None] for which in range(4)]
    turned_back = results[4]
    landed = lax.all_to_all(turned_back, "mp", split_axis=1, concat_axis=1, tiled=True)
    landed = landed.reshape(slot_count, owner_count, row_count, block_width)
    moment_new = jnp.einsum(
        "jso,sorc->jrc", onehot, landed, preferred_element_type=jnp.float32
    ).astype(jnp.bfloat16)
    return (stacked[0], stacked[1], stacked[2], stacked[3], moment_new)


DP = ("dpo", "dpi")


def solution(mesh):
    dp_count, mp_count = mesh.shape["dp"], mesh.shape["mp"]
    inner = 2 if dp_count % 2 == 0 else 1
    split_mesh = jax.sharding.Mesh(
        mesh.devices.reshape(dp_count // inner, inner, mp_count), ("dpo", "dpi", "mp")
    )
    return jax.shard_map(
        local,
        mesh=split_mesh,
        in_specs=(
            P(DP, None, "mp", None),
            P(),
            P(DP, "mp", None),
            P(DP, "mp", None, None, None),
            P(DP, "mp", None, None, None),
            P(DP, "mp", None, None, None),
            P(DP, "mp", None, None, None),
        ),
        out_specs=(
            P(DP, "mp", None, None, None),
            P(DP, "mp", None, None, None),
            P(DP, "mp", None, None, None),
            P(DP, "mp", None, None, None),
            P(DP, "mp", None),
        ),
        check_vma=False,
    )
```

```python
import functools

import jax
import jax.numpy as jnp
from jax import lax
from jax.experimental import pallas as pl
from jax.experimental.pallas import tpu as pltpu
from jax.sharding import PartitionSpec as P

gram_decay = 0.85
moment_decay = 0.9


def slot_numbers(row):
    length = row.shape[0]
    equal_owner = row[:, None] == row[None, :]
    earlier = lax.broadcasted_iota(jnp.int32, (length, length), 1) < lax.broadcasted_iota(
        jnp.int32, (length, length), 0
    )
    return jnp.sum(jnp.where(equal_owner & earlier, 1, 0), axis=1).astype(jnp.int32)


def slot_mapping(row, slot_count, owner_count):
    numbers = slot_numbers(row)
    by_owner = row[:, None, None] == lax.broadcasted_iota(jnp.int32, (1, 1, owner_count), 2)
    by_slot = numbers[:, None, None] == lax.broadcasted_iota(jnp.int32, (1, slot_count, 1), 1)
    return (by_owner & by_slot).astype(jnp.bfloat16)


def pack_rows(onehot, rows_in):
    spread = jnp.einsum("jso,jrc->sorc", onehot, rows_in, preferred_element_type=jnp.float32)
    return spread.astype(jnp.bfloat16).reshape(
        spread.shape[0], spread.shape[1] * spread.shape[2], spread.shape[3]
    )


HI = lax.Precision.HIGHEST

def _nt(a, b, precision=HI):
    return lax.dot_general(a, b, (((1,), (1,)), ((), ())), precision=precision,
                           preferred_element_type=jnp.float32)

def _orth_kernel(s_ref, p_ref, q_ref, a_ref, m_ref, w_ref, qf_ref, *, nb):
    bsz, n, _ = s_ref.shape
    kb = n // nb
    a_ref[...] = s_ref[...]
    lane_l = lax.broadcasted_iota(jnp.int32, (1, 1, nb), 2)
    for k in range(kb):
        k0 = k * nb
        m_ref[...] = a_ref[:, k0:k0 + nb, k0:k0 + nb]
        for t in range(nb // 8):
            r0 = 8 * t
            sub = lax.broadcasted_iota(jnp.int32, (1, nb - r0, 1), 1) + r0

            def step(jj, carry, r0=r0, sub=sub):
                j = r0 + jj
                row = m_ref[:, pl.ds(j, 1), :]
                at_j = lane_l == j
                piv = jnp.sum(jnp.where(at_j, row, 0.0), axis=-1, keepdims=True)
                inv_s = lax.rsqrt(piv)
                scaled = jnp.where(at_j, inv_s, row * inv_s)
                blk = m_ref[:, r0:, :]
                below = sub > j
                col = jnp.sum(jnp.where(at_j, blk, 0.0), axis=-1, keepdims=True) * inv_s
                col = jnp.where(below, col, 0.0)
                blk = jnp.where(at_j & below, 0.0, blk) - col * scaled
                m_ref[:, r0:, :] = blk
                m_ref[:, pl.ds(j, 1), :] = scaled
                return carry

            lax.fori_loop(0, 8, step, 0, unroll=True)
        low = (lax.broadcasted_iota(jnp.int32, (1, nb, nb), 2)
               <= lax.broadcasted_iota(jnp.int32, (1, nb, nb), 1))
        w_ref[:, k] = jnp.where(low, m_ref[...], 0.0)
        if k < kb - 1:
            for b in range(bsz):
                panel = _nt(a_ref[b, k0 + nb:, k0:k0 + nb], w_ref[b, k])
                a_ref[b, k0 + nb:, k0:k0 + nb] = panel
                a_ref[b, k0 + nb:, k0 + nb:] = a_ref[b, k0 + nb:, k0 + nb:] - _nt(panel, panel)
    for k in range(kb):
        k0 = k * nb
        for b in range(bsz):
            rhs = p_ref[b, :, k0:k0 + nb]
            if k > 0:
                rhs = rhs - _nt(qf_ref[b, :, :k0], a_ref[b, k0:k0 + nb, :k0], lax.Precision.HIGH)
            qf_ref[b, :, k0:k0 + nb] = _nt(rhs, w_ref[b, k], lax.Precision.HIGH)
    q_ref[...] = qf_ref[...].astype(q_ref.dtype)


def orth_batch(square, power, nb=128):
    bsz, n, _ = square.shape
    vmem = pltpu.VMEM
    return pl.pallas_call(
        functools.partial(_orth_kernel, nb=nb),
        out_shape=jax.ShapeDtypeStruct((bsz, n, n), jnp.bfloat16),
        in_specs=[pl.BlockSpec(memory_space=vmem)] * 2,
        out_specs=pl.BlockSpec(memory_space=vmem),
        scratch_shapes=[
            vmem((bsz, n, n), jnp.float32),
            vmem((bsz, nb, nb), jnp.float32),
            vmem((bsz, n // nb, nb, nb), jnp.float32),
            vmem((bsz, n, n), jnp.float32),
        ],
        compiler_params=pltpu.CompilerParams(vmem_limit_bytes=60 * 1024 * 1024),
    )(square, power)


def refresh_all(left_gram, right_gram, left_old, right_old, gradient, moment):
    block_width = gradient.shape[-1]
    slots = gradient.shape[0]
    outer_left = jnp.einsum("sij,skj->sik", gradient, gradient, preferred_element_type=jnp.float32)
    outer_right = jnp.einsum("sji,sjk->sik", gradient, gradient, preferred_element_type=jnp.float32)
    left_stat = (
        gram_decay * left_gram.astype(jnp.float32) + (1.0 - gram_decay) / block_width * outer_left
    ).astype(jnp.bfloat16)
    right_statistic = (
        gram_decay * right_gram.astype(jnp.float32) + (1.0 - gram_decay) / block_width * outer_right
    ).astype(jnp.bfloat16)
    left_power = jnp.einsum("sij,sjk->sik", left_stat, left_old, preferred_element_type=jnp.float32)
    right_power = jnp.einsum(
        "sij,sjk->sik", right_statistic, right_old, preferred_element_type=jnp.float32
    )
    power = jnp.concatenate([left_power, right_power], axis=0)
    square = jnp.einsum(
        "bji,bjk->bik", power, power, precision=lax.Precision.HIGHEST,
        preferred_element_type=jnp.float32,
    )
    basis = orth_batch(square, power)
    left_basis, right_basis = basis[:slots], basis[slots:]
    restored = jnp.einsum(
        "sij,sjk->sik", left_old, moment, preferred_element_type=jnp.float32
    ).astype(jnp.bfloat16)
    mixed = (
        moment_decay
        * jnp.einsum("sij,skj->sik", restored, right_old, preferred_element_type=jnp.float32)
        + (1.0 - moment_decay) * gradient.astype(jnp.float32)
    ).astype(jnp.bfloat16)
    turned = jnp.einsum(
        "sji,sjk->sik", left_basis, mixed, preferred_element_type=jnp.float32
    ).astype(jnp.bfloat16)
    moment_new = jnp.einsum(
        "sij,sjk->sik", turned, right_basis, preferred_element_type=jnp.float32
    ).astype(jnp.bfloat16)
    return (left_stat, right_statistic, left_basis, right_basis, moment_new)


def local(grad_part, owner, moment, gram_left, gram_right, basis_left, basis_right):
    owner_count = lax.axis_size("mp")
    my_index = lax.axis_index("mp")
    my_group = lax.axis_index("dp")
    row_count = moment.shape[1]
    block_width = moment.shape[2]
    slot_count = gram_left.shape[2]
    my_table = lax.dynamic_index_in_dim(owner, my_group, 0, keepdims=False)
    onehot = slot_mapping(my_table, slot_count, owner_count)
    replica_count = lax.axis_size("dp")
    parts = lax.all_to_all(grad_part[0], "dp", split_axis=0, concat_axis=0, tiled=True)
    parts = parts.reshape((replica_count, -1) + parts.shape[1:])
    total = jnp.zeros(parts.shape[1:], jnp.float32)
    for replica in range(replica_count):
        total = total + parts[replica].astype(jnp.float32)
    summed = total.astype(jnp.bfloat16)
    grads, moments = (
        lax.all_to_all(pack_rows(onehot, summed), "mp", split_axis=1, concat_axis=1, tiled=True),
        lax.all_to_all(pack_rows(onehot, moment), "mp", split_axis=1, concat_axis=1, tiled=True),
    )
    my_load = jnp.sum(jnp.where(my_table == my_index, 1, 0))
    results = refresh_all(
        gram_left[0, 0], gram_right[0, 0], basis_left[0, 0], basis_right[0, 0], grads, moments
    )
    live = (lax.broadcasted_iota(jnp.int32, (slot_count, 1, 1), 0) < my_load)
    results = [jnp.where(live, r, jnp.zeros_like(r)) for r in results]
    stacked = [results[which][None, None] for which in range(4)]
    turned_back = results[4]
    landed = lax.all_to_all(turned_back, "mp", split_axis=1, concat_axis=1, tiled=True)
    landed = landed.reshape(slot_count, owner_count, row_count, block_width)
    moment_new = jnp.einsum(
        "jso,sorc->jrc", onehot, landed, preferred_element_type=jnp.float32
    ).astype(jnp.bfloat16)
    return (stacked[0], stacked[1], stacked[2], stacked[3], moment_new)


def solution(mesh):
    return jax.shard_map(
        local,
        mesh=mesh,
        in_specs=(
            P("dp", None, "mp", None),
            P(),
            P("dp", "mp", None),
            P("dp", "mp", None, None, None),
            P("dp", "mp", None, None, None),
            P("dp", "mp", None, None, None),
            P("dp", "mp", None, None, None),
        ),
        out_specs=(
            P("dp", "mp", None, None, None),
            P("dp", "mp", None, None, None),
            P("dp", "mp", None, None, None),
            P("dp", "mp", None, None, None),
            P("dp", "mp", None),
        ),
        check_vma=False,
    )
```

```python
import functools

import jax
import jax.numpy as jnp
from jax import lax
from jax.experimental import pallas as pl
from jax.experimental.pallas import tpu as pltpu
from jax.sharding import PartitionSpec as P

gram_decay = 0.85
moment_decay = 0.9


def slot_numbers(row):
    length = row.shape[0]
    equal_owner = row[:, None] == row[None, :]
    earlier = lax.broadcasted_iota(jnp.int32, (length, length), 1) < lax.broadcasted_iota(
        jnp.int32, (length, length), 0
    )
    return jnp.sum(jnp.where(equal_owner & earlier, 1, 0), axis=1).astype(jnp.int32)


def slot_mapping(row, slot_count, owner_count):
    numbers = slot_numbers(row)
    by_owner = row[:, None, None] == lax.broadcasted_iota(jnp.int32, (1, 1, owner_count), 2)
    by_slot = numbers[:, None, None] == lax.broadcasted_iota(jnp.int32, (1, slot_count, 1), 1)
    return (by_owner & by_slot).astype(jnp.bfloat16)


def pack_rows(onehot, rows_in):
    spread = jnp.einsum("jso,jrc->sorc", onehot, rows_in, preferred_element_type=jnp.float32)
    return spread.astype(jnp.bfloat16).reshape(
        spread.shape[0], spread.shape[1] * spread.shape[2], spread.shape[3]
    )


HI = lax.Precision.HIGHEST

def _nt(a, b, precision=HI):
    return lax.dot_general(a, b, (((1,), (1,)), ((), ())), precision=precision,
                           preferred_element_type=jnp.float32)

def _orth_kernel(sl_ref, sr_ref, pl_ref, pr_ref, ql_ref, qr_ref, a_ref, m_ref, w_ref, qf_ref, *, nb):
    half, n, _ = sl_ref.shape
    bsz = 2 * half
    kb = n // nb
    a_ref[:half] = sl_ref[...]
    a_ref[half:] = sr_ref[...]
    lane_l = lax.broadcasted_iota(jnp.int32, (1, 1, nb), 2)
    for k in range(kb):
        k0 = k * nb
        m_ref[...] = a_ref[:, k0:k0 + nb, k0:k0 + nb]
        for t in range(nb // 8):
            r0 = 8 * t
            sub = lax.broadcasted_iota(jnp.int32, (1, nb - r0, 1), 1) + r0

            def step(jj, carry, r0=r0, sub=sub):
                j = r0 + jj
                row = m_ref[:, pl.ds(j, 1), :]
                at_j = lane_l == j
                piv = jnp.sum(jnp.where(at_j, row, 0.0), axis=-1, keepdims=True)
                inv_s = lax.rsqrt(piv)
                scaled = jnp.where(at_j, inv_s, row * inv_s)
                blk = m_ref[:, r0:, :]
                below = sub > j
                col = jnp.sum(jnp.where(at_j, blk, 0.0), axis=-1, keepdims=True) * inv_s
                col = jnp.where(below, col, 0.0)
                blk = jnp.where(at_j & below, 0.0, blk) - col * scaled
                m_ref[:, r0:, :] = blk
                m_ref[:, pl.ds(j, 1), :] = scaled
                return carry

            lax.fori_loop(0, 8, step, 0, unroll=True)
        low = (lax.broadcasted_iota(jnp.int32, (1, nb, nb), 2)
               <= lax.broadcasted_iota(jnp.int32, (1, nb, nb), 1))
        w_ref[:, k] = jnp.where(low, m_ref[...], 0.0)
        if k < kb - 1:
            for b in range(bsz):
                panel = _nt(a_ref[b, k0 + nb:, k0:k0 + nb], w_ref[b, k])
                a_ref[b, k0 + nb:, k0:k0 + nb] = panel
                a_ref[b, k0 + nb:, k0 + nb:] = a_ref[b, k0 + nb:, k0 + nb:] - _nt(panel, panel)
    for k in range(kb):
        k0 = k * nb
        for b in range(bsz):
            rhs = (pl_ref if b < half else pr_ref)[b % half, :, k0:k0 + nb]
            if k > 0:
                rhs = rhs - _nt(qf_ref[b, :, :k0], a_ref[b, k0:k0 + nb, :k0], lax.Precision.HIGH)
            qf_ref[b, :, k0:k0 + nb] = _nt(rhs, w_ref[b, k], lax.Precision.HIGH)
    ql_ref[...] = qf_ref[:half].astype(ql_ref.dtype)
    qr_ref[...] = qf_ref[half:].astype(qr_ref.dtype)


def orth_pair(square_left, square_right, power_left, power_right, nb=128):
    half, n, _ = square_left.shape
    bsz = 2 * half
    vmem = pltpu.VMEM
    return pl.pallas_call(
        functools.partial(_orth_kernel, nb=nb),
        out_shape=[jax.ShapeDtypeStruct((half, n, n), jnp.bfloat16)] * 2,
        in_specs=[pl.BlockSpec(memory_space=vmem)] * 4,
        out_specs=[pl.BlockSpec(memory_space=vmem)] * 2,
        scratch_shapes=[
            vmem((bsz, n, n), jnp.float32),
            vmem((bsz, nb, nb), jnp.float32),
            vmem((bsz, n // nb, nb, nb), jnp.float32),
            vmem((bsz, n, n), jnp.float32),
        ],
        compiler_params=pltpu.CompilerParams(vmem_limit_bytes=60 * 1024 * 1024),
    )(square_left, square_right, power_left, power_right)


def refresh_all(left_gram, right_gram, left_old, right_old, gradient, moment):
    block_width = gradient.shape[-1]
    slots = gradient.shape[0]
    outer_left = jnp.einsum("sij,skj->sik", gradient, gradient, preferred_element_type=jnp.float32)
    outer_right = jnp.einsum("sji,sjk->sik", gradient, gradient, preferred_element_type=jnp.float32)
    left_stat = (
        gram_decay * left_gram.astype(jnp.float32) + (1.0 - gram_decay) / block_width * outer_left
    ).astype(jnp.bfloat16)
    right_statistic = (
        gram_decay * right_gram.astype(jnp.float32) + (1.0 - gram_decay) / block_width * outer_right
    ).astype(jnp.bfloat16)
    left_power = jnp.einsum("sij,sjk->sik", left_stat, left_old, preferred_element_type=jnp.float32)
    right_power = jnp.einsum(
        "sij,sjk->sik", right_statistic, right_old, preferred_element_type=jnp.float32
    )
    square_left, square_right = (
        jnp.einsum(
            "bji,bjk->bik", power, power, precision=lax.Precision.HIGHEST,
            preferred_element_type=jnp.float32,
        )
        for power in (left_power, right_power)
    )
    left_basis, right_basis = orth_pair(square_left, square_right, left_power, right_power)
    restored = jnp.einsum(
        "sij,sjk->sik", left_old, moment, preferred_element_type=jnp.float32
    ).astype(jnp.bfloat16)
    mixed = (
        moment_decay
        * jnp.einsum("sij,skj->sik", restored, right_old, preferred_element_type=jnp.float32)
        + (1.0 - moment_decay) * gradient.astype(jnp.float32)
    ).astype(jnp.bfloat16)
    turned = jnp.einsum(
        "sji,sjk->sik", left_basis, mixed, preferred_element_type=jnp.float32
    ).astype(jnp.bfloat16)
    moment_new = jnp.einsum(
        "sij,sjk->sik", turned, right_basis, preferred_element_type=jnp.float32
    ).astype(jnp.bfloat16)
    return (left_stat, right_statistic, left_basis, right_basis, moment_new)


def local(grad_part, owner, moment, gram_left, gram_right, basis_left, basis_right):
    owner_count = lax.axis_size("mp")
    my_index = lax.axis_index("mp")
    my_group = lax.axis_index("dp")
    row_count = moment.shape[1]
    block_width = moment.shape[2]
    slot_count = gram_left.shape[2]
    my_table = lax.dynamic_index_in_dim(owner, my_group, 0, keepdims=False)
    onehot = slot_mapping(my_table, slot_count, owner_count)
    replica_count = lax.axis_size("dp")
    parts = lax.all_to_all(grad_part[0], "dp", split_axis=0, concat_axis=0, tiled=True)
    parts = parts.reshape((replica_count, -1) + parts.shape[1:])
    total = jnp.zeros(parts.shape[1:], jnp.float32)
    for replica in range(replica_count):
        total = total + parts[replica].astype(jnp.float32)
    summed = total.astype(jnp.bfloat16)
    grads, moments = (
        lax.all_to_all(pack_rows(onehot, summed), "mp", split_axis=1, concat_axis=1, tiled=True),
        lax.all_to_all(pack_rows(onehot, moment), "mp", split_axis=1, concat_axis=1, tiled=True),
    )
    my_load = jnp.sum(jnp.where(my_table == my_index, 1, 0))
    results = refresh_all(
        gram_left[0, 0], gram_right[0, 0], basis_left[0, 0], basis_right[0, 0], grads, moments
    )
    live = (lax.broadcasted_iota(jnp.int32, (slot_count, 1, 1), 0) < my_load)
    results = [jnp.where(live, r, jnp.zeros_like(r)) for r in results]
    stacked = [results[which][None, None] for which in range(4)]
    turned_back = results[4]
    landed = lax.all_to_all(turned_back, "mp", split_axis=1, concat_axis=1, tiled=True)
    landed = landed.reshape(slot_count, owner_count, row_count, block_width)
    moment_new = jnp.einsum(
        "jso,sorc->jrc", onehot, landed, preferred_element_type=jnp.float32
    ).astype(jnp.bfloat16)
    return (stacked[0], stacked[1], stacked[2], stacked[3], moment_new)


def solution(mesh):
    return jax.shard_map(
        local,
        mesh=mesh,
        in_specs=(
            P("dp", None, "mp", None),
            P(),
            P("dp", "mp", None),
            P("dp", "mp", None, None, None),
            P("dp", "mp", None, None, None),
            P("dp", "mp", None, None, None),
            P("dp", "mp", None, None, None),
        ),
        out_specs=(
            P("dp", "mp", None, None, None),
            P("dp", "mp", None, None, None),
            P("dp", "mp", None, None, None),
            P("dp", "mp", None, None, None),
            P("dp", "mp", None),
        ),
        check_vma=False,
    )
```

```python
import functools

import jax
import jax.numpy as jnp
from jax import lax
from jax.experimental import pallas as pl
from jax.experimental.pallas import tpu as pltpu
from jax.sharding import PartitionSpec as P

gram_decay = 0.85
moment_decay = 0.9


def slot_numbers(row):
    length = row.shape[0]
    equal_owner = row[:, None] == row[None, :]
    earlier = lax.broadcasted_iota(jnp.int32, (length, length), 1) < lax.broadcasted_iota(
        jnp.int32, (length, length), 0
    )
    return jnp.sum(jnp.where(equal_owner & earlier, 1, 0), axis=1).astype(jnp.int32)


def slot_mapping(row, slot_count, owner_count):
    numbers = slot_numbers(row)
    by_owner = row[:, None, None] == lax.broadcasted_iota(jnp.int32, (1, 1, owner_count), 2)
    by_slot = numbers[:, None, None] == lax.broadcasted_iota(jnp.int32, (1, slot_count, 1), 1)
    return (by_owner & by_slot).astype(jnp.bfloat16)


def pack_rows(onehot, rows_in):
    spread = jnp.einsum("jso,jrc->sorc", onehot, rows_in, preferred_element_type=jnp.float32)
    return spread.astype(jnp.bfloat16).reshape(
        spread.shape[0], spread.shape[1] * spread.shape[2], spread.shape[3]
    )


HI = lax.Precision.HIGHEST

def _nt(a, b, precision=HI):
    return lax.dot_general(a, b, (((1,), (1,)), ((), ())), precision=precision,
                           preferred_element_type=jnp.float32)

def _orth_kernel(sl_ref, sr_ref, pl_ref, pr_ref, ql_ref, qr_ref, a_ref, m_ref, w_ref, qf_ref, *, nb):
    half, n, _ = sl_ref.shape
    bsz = 2 * half
    kb = n // nb
    a_ref[:half] = sl_ref[...]
    a_ref[half:] = sr_ref[...]
    lane_l = lax.broadcasted_iota(jnp.int32, (1, 1, nb), 2)
    for k in range(kb):
        k0 = k * nb
        m_ref[...] = a_ref[:, k0:k0 + nb, k0:k0 + nb]
        for t in range(nb // 8):
            r0 = 8 * t
            sub = lax.broadcasted_iota(jnp.int32, (1, nb - r0, 1), 1) + r0

            def step(jj, carry, r0=r0, sub=sub):
                j = r0 + jj
                row = m_ref[:, pl.ds(j, 1), :]
                at_j = lane_l == j
                piv = jnp.sum(jnp.where(at_j, row, 0.0), axis=-1, keepdims=True)
                inv_s = lax.rsqrt(piv)
                scaled = jnp.where(at_j, inv_s, row * inv_s)
                blk = m_ref[:, r0:, :]
                below = sub > j
                col = jnp.sum(jnp.where(at_j, blk, 0.0), axis=-1, keepdims=True) * inv_s
                col = jnp.where(below, col, 0.0)
                blk = jnp.where(at_j & below, 0.0, blk) - col * scaled
                m_ref[:, r0:, :] = blk
                m_ref[:, pl.ds(j, 1), :] = scaled
                return carry

            lax.fori_loop(0, 8, step, 0, unroll=True)
        low = (lax.broadcasted_iota(jnp.int32, (1, nb, nb), 2)
               <= lax.broadcasted_iota(jnp.int32, (1, nb, nb), 1))
        w_ref[:, k] = jnp.where(low, m_ref[...], 0.0)
        if k < kb - 1:
            for b in range(bsz):
                panel = _nt(a_ref[b, k0 + nb:, k0:k0 + nb], w_ref[b, k])
                a_ref[b, k0 + nb:, k0:k0 + nb] = panel
                a_ref[b, k0 + nb:, k0 + nb:] = a_ref[b, k0 + nb:, k0 + nb:] - _nt(panel, panel)
    for k in range(kb):
        k0 = k * nb
        for b in range(bsz):
            rhs = (pl_ref if b < half else pr_ref)[b % half, :, k0:k0 + nb]
            if k > 0:
                rhs = rhs - _nt(qf_ref[b, :, :k0], a_ref[b, k0:k0 + nb, :k0], lax.Precision.HIGH)
            qf_ref[b, :, k0:k0 + nb] = _nt(rhs, w_ref[b, k], lax.Precision.HIGH)
    ql_ref[...] = qf_ref[:half].astype(ql_ref.dtype)
    qr_ref[...] = qf_ref[half:].astype(qr_ref.dtype)


def orth_pair(square_left, square_right, power_left, power_right, nb=128):
    half, n, _ = square_left.shape
    bsz = 2 * half
    vmem = pltpu.VMEM
    return pl.pallas_call(
        functools.partial(_orth_kernel, nb=nb),
        out_shape=[jax.ShapeDtypeStruct((half, n, n), jnp.bfloat16)] * 2,
        in_specs=[pl.BlockSpec(memory_space=vmem)] * 4,
        out_specs=[pl.BlockSpec(memory_space=vmem)] * 2,
        scratch_shapes=[
            vmem((bsz, n, n), jnp.float32),
            vmem((bsz, nb, nb), jnp.float32),
            vmem((bsz, n // nb, nb, nb), jnp.float32),
            vmem((bsz, n, n), jnp.float32),
        ],
        compiler_params=pltpu.CompilerParams(vmem_limit_bytes=60 * 1024 * 1024),
    )(square_left, square_right, power_left, power_right)


def refresh_all(left_gram, right_gram, left_old, right_old, gradient, moment):
    block_width = gradient.shape[-1]
    slots = gradient.shape[0]
    outer_left = jnp.einsum("sij,skj->sik", gradient, gradient, preferred_element_type=jnp.float32)
    outer_right = jnp.einsum("sji,sjk->sik", gradient, gradient, preferred_element_type=jnp.float32)
    left_stat = (
        gram_decay * left_gram.astype(jnp.float32) + (1.0 - gram_decay) / block_width * outer_left
    ).astype(jnp.bfloat16)
    right_statistic = (
        gram_decay * right_gram.astype(jnp.float32) + (1.0 - gram_decay) / block_width * outer_right
    ).astype(jnp.bfloat16)
    left_power = jnp.einsum("sij,sjk->sik", left_stat, left_old, preferred_element_type=jnp.float32)
    right_power = jnp.einsum(
        "sij,sjk->sik", right_statistic, right_old, preferred_element_type=jnp.float32
    )
    square_left, square_right = (
        jnp.einsum(
            "bji,bjk->bik", power, power, precision=lax.Precision.HIGHEST,
            preferred_element_type=jnp.float32,
        )
        for power in (left_power, right_power)
    )
    left_basis, right_basis = orth_pair(square_left, square_right, left_power, right_power)
    restored = jnp.einsum(
        "sij,sjk->sik", left_old, moment, preferred_element_type=jnp.float32
    ).astype(jnp.bfloat16)
    mixed = (
        moment_decay
        * jnp.einsum("sij,skj->sik", restored, right_old, preferred_element_type=jnp.float32)
        + (1.0 - moment_decay) * gradient.astype(jnp.float32)
    ).astype(jnp.bfloat16)
    turned = jnp.einsum(
        "sji,sjk->sik", left_basis, mixed, preferred_element_type=jnp.float32
    ).astype(jnp.bfloat16)
    moment_new = jnp.einsum(
        "sij,sjk->sik", turned, right_basis, preferred_element_type=jnp.float32
    ).astype(jnp.bfloat16)
    return (left_stat, right_statistic, left_basis, right_basis, moment_new)


def local(grad_part, owner, moment, gram_left, gram_right, basis_left, basis_right):
    owner_count = lax.axis_size("mp")
    my_index = lax.axis_index("mp")
    my_group = lax.axis_index("dp")
    row_count = moment.shape[1]
    block_width = moment.shape[2]
    slot_count = gram_left.shape[2]
    my_table = lax.dynamic_index_in_dim(owner, my_group, 0, keepdims=False)
    onehot = slot_mapping(my_table, slot_count, owner_count)
    replica_count = lax.axis_size("dp")
    parts = lax.all_to_all(grad_part[0], "dp", split_axis=0, concat_axis=0, tiled=True)
    parts = parts.reshape((replica_count, -1) + parts.shape[1:])
    total = jnp.zeros(parts.shape[1:], jnp.float32)
    for replica in range(replica_count):
        total = total + parts[replica].astype(jnp.float32)
    summed = total.astype(jnp.bfloat16)
    grads, moments = (
        lax.all_to_all(pack_rows(onehot, summed), "mp", split_axis=1, concat_axis=1, tiled=True),
        lax.all_to_all(pack_rows(onehot, moment), "mp", split_axis=1, concat_axis=1, tiled=True),
    )
    my_load = jnp.sum(jnp.where(my_table == my_index, 1, 0))
    results = refresh_all(
        gram_left[0, 0], gram_right[0, 0], basis_left[0, 0], basis_right[0, 0], grads, moments
    )
    live = (lax.broadcasted_iota(jnp.int32, (slot_count, 1, 1), 0) < my_load)
    results = [jnp.where(live, r, jnp.zeros_like(r)) for r in results]
    stacked = [results[which][None, None] for which in range(4)]
    turned_back = results[4]
    landed = lax.all_to_all(turned_back, "mp", split_axis=1, concat_axis=1, tiled=True)
    landed = landed.reshape(slot_count, owner_count, row_count, block_width)
    chosen = onehot[:, :, :, None, None] > 0
    moment_new = jnp.sum(
        jnp.where(chosen, landed[None], jnp.zeros_like(landed[None])), axis=(1, 2)
    )
    return (stacked[0], stacked[1], stacked[2], stacked[3], moment_new)


def solution(mesh):
    return jax.shard_map(
        local,
        mesh=mesh,
        in_specs=(
            P("dp", None, "mp", None),
            P(),
            P("dp", "mp", None),
            P("dp", "mp", None, None, None),
            P("dp", "mp", None, None, None),
            P("dp", "mp", None, None, None),
            P("dp", "mp", None, None, None),
        ),
        out_specs=(
            P("dp", "mp", None, None, None),
            P("dp", "mp", None, None, None),
            P("dp", "mp", None, None, None),
            P("dp", "mp", None, None, None),
            P("dp", "mp", None),
        ),
        check_vma=False,
    )
```

```python
import functools

import jax
import jax.numpy as jnp
from jax import lax
from jax.experimental import pallas as pl
from jax.experimental.pallas import tpu as pltpu
from jax.sharding import PartitionSpec as P

gram_decay = 0.85
moment_decay = 0.9


def slot_numbers(row):
    length = row.shape[0]
    equal_owner = row[:, None] == row[None, :]
    earlier = lax.broadcasted_iota(jnp.int32, (length, length), 1) < lax.broadcasted_iota(
        jnp.int32, (length, length), 0
    )
    return jnp.sum(jnp.where(equal_owner & earlier, 1, 0), axis=1).astype(jnp.int32)


def slot_mapping(row, slot_count, owner_count):
    numbers = slot_numbers(row)
    by_owner = row[:, None, None] == lax.broadcasted_iota(jnp.int32, (1, 1, owner_count), 2)
    by_slot = numbers[:, None, None] == lax.broadcasted_iota(jnp.int32, (1, slot_count, 1), 1)
    return (by_owner & by_slot).astype(jnp.bfloat16)


def pack_rows(onehot, rows_in):
    spread = jnp.einsum("jso,jrc->sorc", onehot, rows_in, preferred_element_type=jnp.float32)
    return spread.astype(jnp.bfloat16).reshape(
        spread.shape[0], spread.shape[1] * spread.shape[2], spread.shape[3]
    )


HI = lax.Precision.HIGHEST

def _nt(a, b, precision=HI):
    return lax.dot_general(a, b, (((1,), (1,)), ((), ())), precision=precision,
                           preferred_element_type=jnp.float32)

def _orth_kernel(sl_ref, sr_ref, pl_ref, pr_ref, ql_ref, qr_ref, a_ref, m_ref, w_ref, qf_ref, *, nb):
    half, n, _ = sl_ref.shape
    bsz = 2 * half
    kb = n // nb
    a_ref[:half] = sl_ref[...]
    a_ref[half:] = sr_ref[...]
    lane_l = lax.broadcasted_iota(jnp.int32, (1, 1, nb), 2)
    for k in range(kb):
        k0 = k * nb
        m_ref[...] = a_ref[:, k0:k0 + nb, k0:k0 + nb]
        for t in range(nb // 8):
            r0 = 8 * t
            sub = lax.broadcasted_iota(jnp.int32, (1, nb - r0, 1), 1) + r0

            def step(jj, carry, r0=r0, sub=sub):
                j = r0 + jj
                row = m_ref[:, pl.ds(j, 1), :]
                at_j = lane_l == j
                piv = jnp.sum(jnp.where(at_j, row, 0.0), axis=-1, keepdims=True)
                inv_s = lax.rsqrt(piv)
                scaled = jnp.where(at_j, inv_s, row * inv_s)
                blk = m_ref[:, r0:, :]
                below = sub > j
                col = jnp.sum(jnp.where(at_j, blk, 0.0), axis=-1, keepdims=True) * inv_s
                col = jnp.where(below, col, 0.0)
                blk = jnp.where(at_j & below, 0.0, blk) - col * scaled
                m_ref[:, r0:, :] = blk
                m_ref[:, pl.ds(j, 1), :] = scaled
                return carry

            lax.fori_loop(0, 8, step, 0, unroll=True)
        low = (lax.broadcasted_iota(jnp.int32, (1, nb, nb), 2)
               <= lax.broadcasted_iota(jnp.int32, (1, nb, nb), 1))
        w_ref[:, k] = jnp.where(low, m_ref[...], 0.0)
        if k < kb - 1:
            for b in range(bsz):
                panel = _nt(a_ref[b, k0 + nb:, k0:k0 + nb], w_ref[b, k])
                a_ref[b, k0 + nb:, k0:k0 + nb] = panel
                for i in range(k + 1, kb):
                    lo, hi = (i - k - 1) * nb, (i - k) * nb
                    a_ref[b, i * nb:(i + 1) * nb, k0 + nb:(i + 1) * nb] = (
                        a_ref[b, i * nb:(i + 1) * nb, k0 + nb:(i + 1) * nb]
                        - _nt(panel[lo:hi], panel[:hi])
                    )
    for k in range(kb):
        k0 = k * nb
        for b in range(bsz):
            rhs = (pl_ref if b < half else pr_ref)[b % half, :, k0:k0 + nb]
            if k > 0:
                rhs = rhs - _nt(qf_ref[b, :, :k0], a_ref[b, k0:k0 + nb, :k0], lax.Precision.HIGH)
            qf_ref[b, :, k0:k0 + nb] = _nt(rhs, w_ref[b, k], lax.Precision.HIGH)
    ql_ref[...] = qf_ref[:half].astype(ql_ref.dtype)
    qr_ref[...] = qf_ref[half:].astype(qr_ref.dtype)


def orth_pair(square_left, square_right, power_left, power_right, nb=128):
    half, n, _ = square_left.shape
    bsz = 2 * half
    vmem = pltpu.VMEM
    return pl.pallas_call(
        functools.partial(_orth_kernel, nb=nb),
        out_shape=[jax.ShapeDtypeStruct((half, n, n), jnp.bfloat16)] * 2,
        in_specs=[pl.BlockSpec(memory_space=vmem)] * 4,
        out_specs=[pl.BlockSpec(memory_space=vmem)] * 2,
        scratch_shapes=[
            vmem((bsz, n, n), jnp.float32),
            vmem((bsz, nb, nb), jnp.float32),
            vmem((bsz, n // nb, nb, nb), jnp.float32),
            vmem((bsz, n, n), jnp.float32),
        ],
        compiler_params=pltpu.CompilerParams(vmem_limit_bytes=60 * 1024 * 1024),
    )(square_left, square_right, power_left, power_right)


def refresh_all(left_gram, right_gram, left_old, right_old, gradient, moment):
    block_width = gradient.shape[-1]
    slots = gradient.shape[0]
    outer_left = jnp.einsum("sij,skj->sik", gradient, gradient, preferred_element_type=jnp.float32)
    outer_right = jnp.einsum("sji,sjk->sik", gradient, gradient, preferred_element_type=jnp.float32)
    left_stat = (
        gram_decay * left_gram.astype(jnp.float32) + (1.0 - gram_decay) / block_width * outer_left
    ).astype(jnp.bfloat16)
    right_statistic = (
        gram_decay * right_gram.astype(jnp.float32) + (1.0 - gram_decay) / block_width * outer_right
    ).astype(jnp.bfloat16)
    left_power = jnp.einsum("sij,sjk->sik", left_stat, left_old, preferred_element_type=jnp.float32)
    right_power = jnp.einsum(
        "sij,sjk->sik", right_statistic, right_old, preferred_element_type=jnp.float32
    )
    square_left, square_right = (
        jnp.einsum(
            "bji,bjk->bik", power, power, precision=lax.Precision.HIGHEST,
            preferred_element_type=jnp.float32,
        )
        for power in (left_power, right_power)
    )
    left_basis, right_basis = orth_pair(square_left, square_right, left_power, right_power)
    restored = jnp.einsum(
        "sij,sjk->sik", left_old, moment, preferred_element_type=jnp.float32
    ).astype(jnp.bfloat16)
    mixed = (
        moment_decay
        * jnp.einsum("sij,skj->sik", restored, right_old, preferred_element_type=jnp.float32)
        + (1.0 - moment_decay) * gradient.astype(jnp.float32)
    ).astype(jnp.bfloat16)
    turned = jnp.einsum(
        "sji,sjk->sik", left_basis, mixed, preferred_element_type=jnp.float32
    ).astype(jnp.bfloat16)
    moment_new = jnp.einsum(
        "sij,sjk->sik", turned, right_basis, preferred_element_type=jnp.float32
    ).astype(jnp.bfloat16)
    return (left_stat, right_statistic, left_basis, right_basis, moment_new)


def local(grad_part, owner, moment, gram_left, gram_right, basis_left, basis_right):
    owner_count = lax.axis_size("mp")
    my_index = lax.axis_index("mp")
    my_group = lax.axis_index("dp")
    row_count = moment.shape[1]
    block_width = moment.shape[2]
    slot_count = gram_left.shape[2]
    my_table = lax.dynamic_index_in_dim(owner, my_group, 0, keepdims=False)
    onehot = slot_mapping(my_table, slot_count, owner_count)
    replica_count = lax.axis_size("dp")
    parts = lax.all_to_all(grad_part[0], "dp", split_axis=0, concat_axis=0, tiled=True)
    parts = parts.reshape((replica_count, -1) + parts.shape[1:])
    total = jnp.zeros(parts.shape[1:], jnp.float32)
    for replica in range(replica_count):
        total = total + parts[replica].astype(jnp.float32)
    summed = total.astype(jnp.bfloat16)
    grads, moments = (
        lax.all_to_all(pack_rows(onehot, summed), "mp", split_axis=1, concat_axis=1, tiled=True),
        lax.all_to_all(pack_rows(onehot, moment), "mp", split_axis=1, concat_axis=1, tiled=True),
    )
    my_load = jnp.sum(jnp.where(my_table == my_index, 1, 0))
    results = refresh_all(
        gram_left[0, 0], gram_right[0, 0], basis_left[0, 0], basis_right[0, 0], grads, moments
    )
    live = (lax.broadcasted_iota(jnp.int32, (slot_count, 1, 1), 0) < my_load)
    results = [jnp.where(live, r, jnp.zeros_like(r)) for r in results]
    stacked = [results[which][None, None] for which in range(4)]
    turned_back = results[4]
    landed = lax.all_to_all(turned_back, "mp", split_axis=1, concat_axis=1, tiled=True)
    landed = landed.reshape(slot_count, owner_count, row_count, block_width)
    moment_new = jnp.einsum(
        "jso,sorc->jrc", onehot, landed, preferred_element_type=jnp.float32
    ).astype(jnp.bfloat16)
    return (stacked[0], stacked[1], stacked[2], stacked[3], moment_new)


def solution(mesh):
    return jax.shard_map(
        local,
        mesh=mesh,
        in_specs=(
            P("dp", None, "mp", None),
            P(),
            P("dp", "mp", None),
            P("dp", "mp", None, None, None),
            P("dp", "mp", None, None, None),
            P("dp", "mp", None, None, None),
            P("dp", "mp", None, None, None),
        ),
        out_specs=(
            P("dp", "mp", None, None, None),
            P("dp", "mp", None, None, None),
            P("dp", "mp", None, None, None),
            P("dp", "mp", None, None, None),
            P("dp", "mp", None),
        ),
        check_vma=False,
    )
```
